256 devices in a mesh: depth: 16 (over y_hi, z), filt: 16 (over x, y_lo, core).
Axes of the slice: x: 4, y: 4 (y_hi: 2, y_lo: 2; y = y_hi * 2 + y_lo), z: 8, core: 2. Of those that a mesh axis runs over, the one named last changes fastest.
Arguments:
- features: bfloat16 [32, 128, 4096], P('depth', 'filt'), may hold values from -6 to 6
- first_kernel: bfloat16 [3, 3, 3, 256, 128], P(None, None, None, 'filt'), may hold values from -0.109375 to 0.109375
- first_bias: float32 [256], P('filt'), may hold values from -1.5 to 1.5
- second_kernel: bfloat16 [3, 3, 3, 256, 256], P(None, None, None, 'filt'), may hold values from -0.078125 to 0.078125
- second_bias: float32 [256], P('filt'), may hold values from -1.5 to 1.5
Outputs:
- activated: bfloat16 [32, 256, 4096], P('depth', 'filt')
The draws below stay inside these ranges and needn't reach their ends.
All inputs are finite; a program needn't handle non-finite values.
Results may differ from the reference program's by a relative error of at most 0.0047.
Values may be sent and summed in bfloat16 or wider, within the bound.
No kernel may reach another device: no remote copies, remote signals or barrier semaphores. Data moves between devices by JAX's collectives and lax.ppermute only.
A program may use at most 64 MiB of HBM per device.

```python
import jax
import jax.numpy as jnp
from jax import lax

CIN = 128
CMID = 256
COUT = 256
SIDE = 64
DEPTH_CELLS = 32
PLANE_CELLS = 4096


def levels(rng, dims, split, smallest, largest):
    factor_of, own = 1.0, jax.random.fold_in(rng, 6)
    for dim, parts in split:
        steps = jnp.exp(jax.random.uniform(jax.random.fold_in(own, dim), (parts,), jnp.float32, smallest / len(split), largest / len(split)))
        factor_of = factor_of * jnp.repeat(steps, dims[dim] // parts).reshape([-1 if axis == dim else 1 for axis in range(len(dims))])
    return factor_of


def normal_values(own_key, extent, spread, bound, pieces=(), held_as=jnp.bfloat16):
    level = levels(own_key, extent, pieces, -0.22, 0.18) if pieces else 1.0
    values = jax.random.normal(own_key, extent, jnp.float32) * spread * level
    return jnp.minimum(jnp.maximum(values, -bound), bound).astype(held_as)


def setup_inputs(seed: int = 0) -> dict:
    keys = jax.random.split(jax.random.key(seed), 6)
    return {
        "features": normal_values(keys[0], (DEPTH_CELLS, CIN, PLANE_CELLS), 1.0, 6.0, ((0, 16), (1, 16))),
        "first_kernel": normal_values(keys[1], (3, 3, 3, CMID, CIN), (27 * CIN) ** -0.5, 0.109375, ((3, 16),)),
        "first_bias": normal_values(keys[2], (CMID,), 0.3, 1.5, ((0, 16),), jnp.float32),
        "second_kernel": normal_values(keys[3], (3, 3, 3, COUT, CMID), (27 * CMID) ** -0.5, 0.078125, ((3, 16),)),
        "second_bias": normal_values(keys[4], (COUT,), 0.3, 1.5, ((0, 16),), jnp.float32),
    }


leak_slope = 0.3


def convolve(volume_in, kernel):
    planes = volume_in.shape[0]
    channels = volume_in.shape[1]
    cube = volume_in.astype(jnp.float32).reshape(planes, channels, SIDE, SIDE)
    left_side = jnp.transpose(cube, (0, 2, 3, 1))[None]
    right_side = jnp.transpose(kernel.astype(jnp.float32), (0, 1, 2, 4, 3))
    result = lax.conv_general_dilated(left_side, right_side, (1, 1, 1), ((1, 1), (1, 1), (1, 1)), dimension_numbers=("NDHWC", "DHWIO", "NDHWC"), precision=lax.Precision.HIGHEST)
    result = jnp.transpose(result[0], (0, 3, 1, 2))
    return result.reshape(planes, kernel.shape[3], SIDE * SIDE)


def activate(summed, bias):
    shifted = summed + bias.astype(jnp.float32)[None, :, None]
    return jnp.where(shifted > 0, shifted, leak_slope * shifted).astype(jnp.bfloat16)


def reference(features, first_kernel, first_bias, second_kernel, second_bias):
    hidden = activate(convolve(features, first_kernel), first_bias)
    return activate(convolve(hidden, second_kernel), second_bias)
```

```python
import jax
import jax.numpy as jnp
from jax import lax
from jax.sharding import PartitionSpec as P

SIDE = 64


leak_slope = 0.3


def tap_products(block, kernel):
    outs, chans = kernel.shape[3], kernel.shape[4]
    taps = kernel.reshape(27 * outs, chans)
    products = jnp.einsum("tc,pcq->tpq", taps, block, preferred_element_type=jnp.float32)
    return products.reshape(3, 3, 3, outs, block.shape[0], block.shape[2])


def spatial_sum(part):
    cells = part.shape[-1]
    column = jnp.arange(cells, dtype=jnp.int32) % SIDE
    reach = SIDE + 1
    framed = jnp.pad(part, ((0, 0), (0, 0), (0, 0), (reach, reach)))
    total = None
    for tap_h in range(3):
        for tap_w in range(3):
            begin = reach + (tap_h - 1) * SIDE + (tap_w - 1)
            window = framed[tap_h, tap_w, :, begin : begin + cells]
            moved = column + (tap_w - 1)
            usable = (moved >= 0) & (moved < SIDE)
            window = jnp.where(usable[None, :], window, jnp.zeros_like(window))
            total = window if total is None else total + window
    return total


def conv_sum(block, kernel):
    planes = block.shape[0]
    products = tap_products(block, kernel)
    count = lax.axis_size("depth")
    forward = [(i, i + 1) for i in range(count - 1)]
    backward = [(i + 1, i) for i in range(count - 1)]
    to_above = spatial_sum(products[0, :, :, :, planes - 1])
    to_below = spatial_sum(products[2, :, :, :, 0])
    from_below = lax.ppermute(to_above, "depth", forward)
    from_above = lax.ppermute(to_below, "depth", backward)
    rows = []
    for plane in range(planes):
        total = None
        for tap_d in range(3):
            source = plane + tap_d - 1
            if 0 <= source < planes:
                piece = spatial_sum(products[tap_d, :, :, :, source])
                total = piece if total is None else total + piece
        if plane == 0:
            total = total + from_below
        if plane == planes - 1:
            total = total + from_above
        rows.append(total)
    return jnp.stack(rows)


def activate(summed, bias):
    shifted = summed + bias[None, :, None]
    return jnp.where(shifted > 0, shifted, leak_slope * shifted).astype(jnp.bfloat16)


def local(features, first_kernel, first_bias, second_kernel, second_bias):
    whole_in = lax.all_gather(features, "filt", axis=1, tiled=True)
    hidden = activate(conv_sum(whole_in, first_kernel), first_bias)
    whole_mid = lax.all_gather(hidden, "filt", axis=1, tiled=True)
    return activate(conv_sum(whole_mid, second_kernel), second_bias)


def solution(mesh):
    in_specs = (
        P("depth", "filt", None),
        P(None, None, None, "filt", None),
        P("filt"),
        P(None, None, None, "filt", None),
        P("filt"),
    )
    out_specs = P("depth", "filt", None)
    return jax.shard_map(local, mesh=mesh, in_specs=in_specs, out_specs=out_specs, check_vma=False)
```

```python
import jax
import jax.numpy as jnp
from jax import lax
from jax.sharding import PartitionSpec as P

SIDE = 64


leak_slope = 0.3


def tap_products(plane, kernel_d):
    outs, chans = kernel_d.shape[2], kernel_d.shape[3]
    taps = kernel_d.reshape(9 * outs, chans)
    products = jnp.einsum("tc,cq->tq", taps, plane, preferred_element_type=jnp.float32)
    return products.reshape(3, 3, outs, plane.shape[1])


def spatial_sum(part):
    cells = part.shape[-1]
    column = jnp.arange(cells, dtype=jnp.int32) % SIDE
    reach = SIDE + 1
    framed = jnp.pad(part, ((0, 0), (0, 0), (0, 0), (reach, reach)))
    total = None
    for tap_h in range(3):
        for tap_w in range(3):
            begin = reach + (tap_h - 1) * SIDE + (tap_w - 1)
            window = framed[tap_h, tap_w, :, begin : begin + cells]
            moved = column + (tap_w - 1)
            usable = (moved >= 0) & (moved < SIDE)
            window = jnp.where(usable[None, :], window, jnp.zeros_like(window))
            total = window if total is None else total + window
    return total


def conv_sum(block, kernel):
    planes = block.shape[0]

    def part(tap_d, source):
        return spatial_sum(tap_products(block[source], kernel[tap_d]))

    count = lax.axis_size("depth")
    forward = [(i, i + 1) for i in range(count - 1)]
    backward = [(i + 1, i) for i in range(count - 1)]
    to_above = part(0, planes - 1)
    to_below = part(2, 0)
    from_below = lax.ppermute(to_above, "depth", forward)
    from_above = lax.ppermute(to_below, "depth", backward)
    rows = []
    for plane in range(planes):
        total = None
        for tap_d in range(3):
            source = plane + tap_d - 1
            if 0 <= source < planes:
                piece = part(tap_d, source)
                total = piece if total is None else total + piece
        if plane == 0:
            total = total + from_below
        if plane == planes - 1:
            total = total + from_above
        rows.append(total)
    return jnp.stack(rows)


def activate(summed, bias):
    shifted = summed + bias[None, :, None]
    return jnp.where(shifted > 0, shifted, leak_slope * shifted).astype(jnp.bfloat16)


def local(features, first_kernel, first_bias, second_kernel, second_bias):
    whole_in = lax.all_gather(features, "filt", axis=1, tiled=True)
    hidden = activate(conv_sum(whole_in, first_kernel), first_bias)
    whole_mid = lax.all_gather(hidden, "filt", axis=1, tiled=True)
    return activate(conv_sum(whole_mid, second_kernel), second_bias)


def solution(mesh):
    in_specs = (
        P("depth", "filt", None),
        P(None, None, None, "filt", None),
        P("filt"),
        P(None, None, None, "filt", None),
        P("filt"),
    )
    out_specs = P("depth", "filt", None)
    return jax.shard_map(local, mesh=mesh, in_specs=in_specs, out_specs=out_specs, check_vma=False)
```

```python
import jax
import jax.numpy as jnp
from jax import lax
from jax.sharding import PartitionSpec as P

SIDE = 64


leak_slope = 0.3


def activate(summed, bias):
    shifted = summed + bias[None, :, None, None]
    return jnp.where(shifted > 0, shifted, leak_slope * shifted).astype(jnp.bfloat16)


def conv(framed, kernel):
    summed = lax.conv_general_dilated(
        framed[None],
        kernel,
        (1, 1, 1),
        ((0, 0), (0, 0), (1, 1)),
        dimension_numbers=("NDCHW", "DHWOI", "NDCHW"),
        preferred_element_type=jnp.float32,
    )
    return summed[0]


def depth_halo(block):
    count = lax.axis_size("depth")
    forward = [(i, i + 1) for i in range(count - 1)]
    backward = [(i + 1, i) for i in range(count - 1)]
    low = lax.ppermute(block[block.shape[0] - 1 :], "depth", forward)
    high = lax.ppermute(block[:1], "depth", backward)
    return jnp.concatenate([low, block, high], axis=0)


def row_halo(block):
    count = lax.axis_size("filt")
    forward = [(i, i + 1) for i in range(count - 1)]
    backward = [(i + 1, i) for i in range(count - 1)]
    above = lax.ppermute(block[:, :, block.shape[2] - 1 :], "filt", forward)
    below = lax.ppermute(block[:, :, :1], "filt", backward)
    return jnp.concatenate([above, block, below], axis=2)


def gather_kernels(first_kernel, second_kernel):
    count = lax.axis_size("filt")
    flat = jnp.concatenate([first_kernel.reshape(-1), second_kernel.reshape(-1)])
    whole = lax.all_gather(flat, "filt", axis=0, tiled=False)
    split = first_kernel.size
    kernels = []
    for part, kernel in ((whole[:, :split], first_kernel), (whole[:, split:], second_kernel)):
        stacked = jnp.moveaxis(part.reshape((count,) + kernel.shape), 0, 3)
        kernels.append(stacked.reshape(3, 3, 3, count * kernel.shape[3], kernel.shape[4]))
    return kernels


def gather_biases(first_bias, second_bias):
    count = lax.axis_size("filt")
    pair = jnp.stack([first_bias, second_bias])
    spread = jnp.broadcast_to(pair[None], (count,) + pair.shape)
    whole = lax.all_to_all(spread, "filt", 0, 0, tiled=True)
    return whole[:, 0].reshape(-1), whole[:, 1].reshape(-1)


def local(features, first_kernel, first_bias, second_kernel, second_bias):
    count = lax.axis_size("filt")
    planes, chans, cells = features.shape
    rows = cells // SIDE
    block_rows = rows // count
    kernel_1, kernel_2 = gather_kernels(first_kernel, second_kernel)
    bias_1, bias_2 = gather_biases(first_bias, second_bias)

    extended = depth_halo(features).reshape(planes + 2, chans, rows, SIDE)
    framed = jnp.pad(extended, ((0, 0), (0, 0), (1, 1), (0, 0)))
    windows = jnp.stack(
        [framed[:, :, b * block_rows : b * block_rows + block_rows + 2] for b in range(count)], axis=2
    )
    windows = windows.reshape(planes + 2, chans, count, (block_rows + 2) * SIDE)
    mine = lax.all_to_all(windows, "filt", 2, 1, tiled=True)
    mine = mine.reshape(planes + 2, count * chans, block_rows + 2, SIDE)

    hidden = activate(conv(mine, kernel_1), bias_1)
    second = activate(conv(row_halo(depth_halo(hidden)), kernel_2), bias_2)

    outs = second_kernel.shape[3]
    second = second.reshape(planes, count, outs, block_rows * SIDE)
    result = lax.all_to_all(second, "filt", 1, 3, tiled=True)
    return result.reshape(planes, outs, cells)


def solution(mesh):
    in_specs = (
        P("depth", "filt", None),
        P(None, None, None, "filt", None),
        P("filt"),
        P(None, None, None, "filt", None),
        P("filt"),
    )
    out_specs = P("depth", "filt", None)
    return jax.shard_map(local, mesh=mesh, in_specs=in_specs, out_specs=out_specs, check_vma=False)
```

```python
import jax
import jax.numpy as jnp
from jax import lax
from jax.sharding import PartitionSpec as P

SIDE = 64


leak_slope = 0.3


def activate(summed, bias):
    shifted = summed + bias[None, :, None, None]
    return jnp.where(shifted > 0, shifted, leak_slope * shifted).astype(jnp.bfloat16)


def conv(framed, kernel):
    summed = lax.conv_general_dilated(
        framed[None],
        kernel,
        (1, 1, 1),
        ((0, 0), (0, 0), (1, 1)),
        dimension_numbers=("NDCHW", "DHWOI", "NDCHW"),
        preferred_element_type=jnp.float32,
    )
    return summed[0]


def depth_halo(block):
    count = lax.axis_size("depth")
    forward = [(i, i + 1) for i in range(count - 1)]
    backward = [(i + 1, i) for i in range(count - 1)]
    low = lax.ppermute(block[block.shape[0] - 1 :], "depth", forward)
    high = lax.ppermute(block[:1], "depth", backward)
    return jnp.concatenate([low, block, high], axis=0)


def full_halo(block):
    depths, parts = lax.axis_size("depth"), lax.axis_size("filt")
    last_plane, last_row = block.shape[0] - 1, block.shape[2] - 1

    def moved(piece, step_d, step_f):
        pairs = []
        for d in range(depths):
            for f in range(parts):
                if 0 <= d + step_d < depths and 0 <= f + step_f < parts:
                    pairs.append((d * parts + f, (d + step_d) * parts + f + step_f))
        return lax.ppermute(piece, ("depth", "filt"), pairs)

    top, bottom = block[last_plane:], block[:1]
    above = moved(block[:, :, last_row:], 0, 1)
    below = moved(block[:, :, :1], 0, -1)
    low = jnp.concatenate(
        [moved(top[:, :, last_row:], 1, 1), moved(top, 1, 0), moved(top[:, :, :1], 1, -1)], axis=2
    )
    high = jnp.concatenate(
        [moved(bottom[:, :, last_row:], -1, 1), moved(bottom, -1, 0), moved(bottom[:, :, :1], -1, -1)], axis=2
    )
    middle = jnp.concatenate([above, block, below], axis=2)
    return jnp.concatenate([low, middle, high], axis=0)


def flat_kernel(whole, kernel):
    count = whole.shape[0]
    stacked = jnp.moveaxis(whole.reshape((count,) + kernel.shape), 0, 3)
    return stacked.reshape(3, 3, 3, count * kernel.shape[3], kernel.shape[4])


def gather_biases(first_bias, second_bias):
    count = lax.axis_size("filt")
    pair = jnp.stack([first_bias, second_bias])
    spread = jnp.broadcast_to(pair[None], (count,) + pair.shape)
    whole = lax.all_to_all(spread, "filt", 0, 0, tiled=True)
    return whole[:, 0].reshape(-1), whole[:, 1].reshape(-1)


def local(features, first_kernel, first_bias, second_kernel, second_bias):
    count = lax.axis_size("filt")
    planes, chans, cells = features.shape
    rows = cells // SIDE
    block_rows = rows // count
    whole_2 = lax.all_gather(second_kernel.reshape(-1), "filt", axis=0, tiled=False)
    bias_1, bias_2 = gather_biases(first_bias, second_bias)

    extended = depth_halo(features).reshape(planes + 2, chans, rows, SIDE)
    framed = jnp.pad(extended, ((0, 0), (0, 0), (1, 1), (0, 0)))
    blocks = framed[:, :, 1 : rows + 1].reshape(planes + 2, chans, count, block_rows, SIDE)
    tops = framed[:, :, 0:rows:block_rows][:, :, :, None]
    bottoms = framed[:, :, block_rows + 1 :: block_rows][:, :, :, None]
    windows = jnp.concatenate([tops, blocks, bottoms], axis=3)
    windows = jnp.moveaxis(windows, 2, 0).reshape(count, -1)
    shard_1 = jnp.broadcast_to(first_kernel.reshape(1, -1), (count, first_kernel.size))
    sent = jnp.concatenate([windows, shard_1], axis=1)
    got = lax.all_to_all(sent, "filt", 0, 0, tiled=True)
    split = windows.shape[1]
    mine = got[:, :split].reshape(count, planes + 2, chans, block_rows + 2, SIDE)
    mine = jnp.moveaxis(mine, 0, 1).reshape(planes + 2, count * chans, block_rows + 2, SIDE)
    kernel_1 = flat_kernel(got[:, split:], first_kernel)

    hidden = activate(conv(mine, kernel_1), bias_1)
    kernel_2 = flat_kernel(whole_2, second_kernel)
    second = activate(conv(full_halo(hidden), kernel_2), bias_2)

    outs = second_kernel.shape[3]
    second = second.reshape(planes, count, outs, block_rows * SIDE)
    result = lax.all_to_all(second, "filt", 1, 3, tiled=True)
    return result.reshape(planes, outs, cells)


def solution(mesh):
    in_specs = (
        P("depth", "filt", None),
        P(None, None, None, "filt", None),
        P("filt"),
        P(None, None, None, "filt", None),
        P("filt"),
    )
    out_specs = P("depth", "filt", None)
    return jax.shard_map(local, mesh=mesh, in_specs=in_specs, out_specs=out_specs, check_vma=False)
```

```python
import jax
import jax.numpy as jnp
from jax import lax
from jax.sharding import PartitionSpec as P

SIDE = 64


leak_slope = 0.3


def activate(summed, bias):
    shifted = summed + bias[None, :, None, None]
    return jnp.where(shifted > 0, shifted, leak_slope * shifted).astype(jnp.bfloat16)


def conv(framed, kernel):
    summed = lax.conv_general_dilated(
        framed[None],
        kernel,
        (1, 1, 1),
        ((0, 0), (0, 0), (1, 1)),
        dimension_numbers=("NDCHW", "ODHWI", "NDCHW"),
        preferred_element_type=jnp.float32,
    )
    return summed[0]


def depth_halo(block, reach):
    count = lax.axis_size("depth")
    forward = [(i, i + 1) for i in range(count - 1)]
    backward = [(i + 1, i) for i in range(count - 1)]
    low = lax.ppermute(block[block.shape[0] - reach :], "depth", forward)
    high = lax.ppermute(block[:reach], "depth", backward)
    return jnp.concatenate([low, block, high], axis=0)


def gather_kernels(first_kernel, second_kernel):
    outs, chans = first_kernel.shape[3], first_kernel.shape[4]
    first = jnp.moveaxis(first_kernel.reshape(27, outs, chans), 1, 0)
    second = jnp.moveaxis(second_kernel.reshape(27, outs, second_kernel.shape[4]), 1, 0)
    whole = lax.all_gather(jnp.concatenate([first, second], axis=2), "filt", axis=0, tiled=True)
    total = whole.shape[0]
    return (
        whole[:, :, :chans].reshape(total, 3, 3, 3, chans),
        whole[:, :, chans:].reshape(total, 3, 3, 3, second_kernel.shape[4]),
    )


def gather_biases(first_bias, second_bias):
    count = lax.axis_size("filt")
    pair = jnp.stack([first_bias, second_bias])
    spread = jnp.broadcast_to(pair[None], (count,) + pair.shape)
    whole = lax.all_to_all(spread, "filt", 0, 0, tiled=True)
    return whole[:, 0].reshape(-1), whole[:, 1].reshape(-1)


def inside(count_planes, count_rows, planes, block_rows):
    plane = lax.axis_index("depth") * planes - 1 + jnp.arange(planes + 2)
    row = lax.axis_index("filt") * block_rows - 1 + jnp.arange(block_rows + 2)
    plane_ok = (plane >= 0) & (plane < count_planes)
    row_ok = (row >= 0) & (row < count_rows)
    return plane_ok[:, None, None, None] & row_ok[None, None, :, None]


def local(features, first_kernel, first_bias, second_kernel, second_bias):
    count = lax.axis_size("filt")
    planes, chans, cells = features.shape
    rows = cells // SIDE
    block_rows = rows // count
    kernel_1, kernel_2 = gather_kernels(first_kernel, second_kernel)
    bias_1, bias_2 = gather_biases(first_bias, second_bias)

    extended = depth_halo(features, 2).reshape(planes + 4, chans, rows, SIDE)
    framed = jnp.pad(extended, ((0, 0), (0, 0), (2, max(2, block_rows)), (0, 0)))
    heads = framed[:, :, :rows].reshape(planes + 4, chans, count, block_rows, SIDE)
    tails = framed[:, :, block_rows : rows + block_rows].reshape(planes + 4, chans, count, block_rows, SIDE)
    windows = jnp.concatenate([heads, tails[:, :, :, : 4]], axis=3)
    windows = windows.reshape(planes + 4, chans, count, (block_rows + 4) * SIDE)
    mine = lax.all_to_all(windows, "filt", 2, 1, tiled=True)
    mine = mine.reshape(planes + 4, count * chans, block_rows + 4, SIDE)

    hidden = activate(conv(mine, kernel_1), bias_1)
    grid = inside(planes * lax.axis_size("depth"), rows, planes, block_rows)
    hidden = jnp.where(grid, hidden, jnp.zeros_like(hidden))
    second = activate(conv(hidden, kernel_2), bias_2)

    outs = second_kernel.shape[3]
    second = second.reshape(planes, count, outs, block_rows * SIDE)
    result = lax.all_to_all(second, "filt", 1, 3, tiled=True)
    return result.reshape(planes, outs, cells)


def solution(mesh):
    in_specs = (
        P("depth", "filt", None),
        P(None, None, None, "filt", None),
        P("filt"),
        P(None, None, None, "filt", None),
        P("filt"),
    )
    out_specs = P("depth", "filt", None)
    return jax.shard_map(local, mesh=mesh, in_specs=in_specs, out_specs=out_specs, check_vma=False)
```

```python
import jax
import jax.numpy as jnp
from jax import lax
from jax.sharding import PartitionSpec as P

SIDE = 64


leak_slope = 0.3


def activate(summed, bias):
    shifted = summed + bias[None, :, None, None]
    return jnp.where(shifted > 0, shifted, leak_slope * shifted).astype(jnp.bfloat16)


def conv(framed, kernel):
    summed = lax.conv_general_dilated(
        framed[None],
        kernel,
        (1, 1, 1),
        ((0, 0), (0, 0), (1, 1)),
        dimension_numbers=("NDCHW", "DHWOI", "NDCHW"),
        preferred_element_type=jnp.float32,
    )
    return summed[0]


def depth_halo(block, reach):
    count = lax.axis_size("depth")
    forward = [(i, i + 1) for i in range(count - 1)]
    backward = [(i + 1, i) for i in range(count - 1)]
    low = lax.ppermute(block[block.shape[0] - reach :], "depth", forward)
    high = lax.ppermute(block[:reach], "depth", backward)
    return jnp.concatenate([low, block, high], axis=0)


def gather_kernels(first_kernel, second_kernel):
    outs, chans = first_kernel.shape[3], first_kernel.shape[4]
    joined = jnp.concatenate(
        [first_kernel.reshape(27, outs, chans), second_kernel.reshape(27, outs, second_kernel.shape[4])], axis=2
    )
    whole = lax.all_gather(joined, "filt", axis=1, tiled=True)
    total = whole.shape[1]
    return (
        whole[:, :, :chans].reshape(3, 3, 3, total, chans),
        whole[:, :, chans:].reshape(3, 3, 3, total, second_kernel.shape[4]),
    )


def gather_biases(first_bias, second_bias):
    count = lax.axis_size("filt")
    pair = jnp.stack([first_bias, second_bias])
    spread = jnp.broadcast_to(pair[None], (count,) + pair.shape)
    whole = lax.all_to_all(spread, "filt", 0, 0, tiled=True)
    return whole[:, 0].reshape(-1), whole[:, 1].reshape(-1)


def inside(count_planes, count_rows, planes, block_rows):
    plane = lax.axis_index("depth") * planes - 1 + jnp.arange(planes + 2)
    row = lax.axis_index("filt") * block_rows - 1 + jnp.arange(block_rows + 2)
    plane_ok = (plane >= 0) & (plane < count_planes)
    row_ok = (row >= 0) & (row < count_rows)
    return plane_ok[:, None, None, None] & row_ok[None, None, :, None]


def local(features, first_kernel, first_bias, second_kernel, second_bias):
    count = lax.axis_size("filt")
    planes, chans, cells = features.shape
    rows = cells // SIDE
    block_rows = rows // count
    kernel_1, kernel_2 = gather_kernels(first_kernel, second_kernel)
    bias_1, bias_2 = gather_biases(first_bias, second_bias)

    extended = depth_halo(features, 2).reshape(planes + 4, chans, rows, SIDE)
    framed = jnp.pad(extended, ((0, 0), (0, 0), (2, max(2, block_rows)), (0, 0)))
    heads = framed[:, :, :rows].reshape(planes + 4, chans, count, block_rows, SIDE)
    tails = framed[:, :, block_rows : rows + block_rows].reshape(planes + 4, chans, count, block_rows, SIDE)
    windows = jnp.concatenate([heads, tails[:, :, :, : 4]], axis=3)
    windows = windows.reshape(planes + 4, chans, count, (block_rows + 4) * SIDE)
    mine = lax.all_to_all(windows, "filt", 2, 1, tiled=True)
    mine = mine.reshape(planes + 4, count * chans, block_rows + 4, SIDE)

    hidden = activate(conv(mine, kernel_1), bias_1)
    grid = inside(planes * lax.axis_size("depth"), rows, planes, block_rows)
    hidden = jnp.where(grid, hidden, jnp.zeros_like(hidden))
    second = activate(conv(hidden, kernel_2), bias_2)

    outs = second_kernel.shape[3]
    second = second.reshape(planes, count, outs, block_rows * SIDE)
    result = lax.all_to_all(second, "filt", 1, 3, tiled=True)
    return result.reshape(planes, outs, cells)


def solution(mesh):
    in_specs = (
        P("depth", "filt", None),
        P(None, None, None, "filt", None),
        P("filt"),
        P(None, None, None, "filt", None),
        P("filt"),
    )
    out_specs = P("depth", "filt", None)
    return jax.shard_map(local, mesh=mesh, in_specs=in_specs, out_specs=out_specs, check_vma=False)
```

```python
import jax
import jax.numpy as jnp
from jax import lax
from jax.sharding import PartitionSpec as P

SIDE = 64


leak_slope = 0.3


def activate(summed, bias):
    shifted = summed + bias[None, :, None, None]
    return jnp.where(shifted > 0, shifted, leak_slope * shifted).astype(jnp.bfloat16)


def conv(framed, kernel):
    summed = lax.conv_general_dilated(
        framed[None],
        kernel,
        (1, 1, 1),
        ((0, 0), (0, 0), (1, 1)),
        dimension_numbers=("NDCHW", "ODHWI", "NDCHW"),
        preferred_element_type=jnp.float32,
    )
    return summed[0]


def depth_halo(block, reach):
    count = lax.axis_size("depth")
    forward = [(i, i + 1) for i in range(count - 1)]
    backward = [(i + 1, i) for i in range(count - 1)]
    low = lax.ppermute(block[block.shape[0] - reach :], "depth", forward)
    high = lax.ppermute(block[:reach], "depth", backward)
    return jnp.concatenate([low, block, high], axis=0)


def gather_kernels(first_kernel, second_kernel):
    outs, chans = first_kernel.shape[3], first_kernel.shape[4]
    first = jnp.moveaxis(first_kernel.reshape(27, outs, chans), 1, 0)
    second = jnp.moveaxis(second_kernel.reshape(27, outs, second_kernel.shape[4]), 1, 0)
    whole = lax.all_gather(jnp.concatenate([first, second], axis=2), "filt", axis=0, tiled=True)
    total = whole.shape[0]
    return (
        whole[:, :, :chans].reshape(total, 3, 3, 3, chans),
        whole[:, :, chans:].reshape(total, 3, 3, 3, second_kernel.shape[4]),
    )


def gather_biases(first_bias, second_bias):
    count = lax.axis_size("filt")
    pair = jnp.stack([first_bias, second_bias])
    spread = jnp.broadcast_to(pair[None], (count,) + pair.shape)
    whole = lax.all_to_all(spread, "filt", 0, 0, tiled=True)
    return whole[:, 0].reshape(-1), whole[:, 1].reshape(-1)


def inside(count_planes, count_rows, planes, block_rows):
    plane = lax.axis_index("depth") * planes - 1 + jnp.arange(planes + 2)
    row = lax.axis_index("filt") * block_rows - 1 + jnp.arange(block_rows + 2)
    plane_ok = (plane >= 0) & (plane < count_planes)
    row_ok = (row >= 0) & (row < count_rows)
    return plane_ok[:, None, None, None] & row_ok[None, None, :, None]


def local(features, first_kernel, first_bias, second_kernel, second_bias):
    count = lax.axis_size("filt")
    planes, chans, cells = features.shape
    rows = cells // SIDE
    block_rows = rows // count
    kernel_1, kernel_2 = gather_kernels(first_kernel, second_kernel)
    bias_1, bias_2 = gather_biases(first_bias, second_bias)

    framed = jnp.pad(features.reshape(planes, chans, rows, SIDE), ((0, 0), (0, 0), (2, max(2, block_rows)), (0, 0)))
    heads = framed[:, :, :rows].reshape(planes, chans, count, block_rows, SIDE)
    tails = framed[:, :, block_rows : rows + block_rows].reshape(planes, chans, count, block_rows, SIDE)
    windows = jnp.concatenate([heads, tails[:, :, :, :4]], axis=3)
    windows = windows.reshape(planes, chans, count, (block_rows + 4) * SIDE)
    mine = lax.all_to_all(windows, "filt", 2, 1, tiled=True)
    mine = depth_halo(mine.reshape(planes, count * chans, block_rows + 4, SIDE), 2)

    hidden = activate(conv(mine, kernel_1), bias_1)
    grid = inside(planes * lax.axis_size("depth"), rows, planes, block_rows)
    hidden = jnp.where(grid, hidden, jnp.zeros_like(hidden))
    second = activate(conv(hidden, kernel_2), bias_2)

    outs = second_kernel.shape[3]
    second = second.reshape(planes, count, outs, block_rows * SIDE)
    result = lax.all_to_all(second, "filt", 1, 3, tiled=True)
    return result.reshape(planes, outs, cells)


def solution(mesh):
    in_specs = (
        P("depth", "filt", None),
        P(None, None, None, "filt", None),
        P("filt"),
        P(None, None, None, "filt", None),
        P("filt"),
    )
    out_specs = P("depth", "filt", None)
    return jax.shard_map(local, mesh=mesh, in_specs=in_specs, out_specs=out_specs, check_vma=False)
```

```python
import jax
import jax.numpy as jnp
from jax import lax
from jax.sharding import PartitionSpec as P

SIDE = 64


leak_slope = 0.3


def activate(summed, bias):
    shifted = summed + bias[None, :, None, None]
    return jnp.where(shifted > 0, shifted, leak_slope * shifted).astype(jnp.bfloat16)


def conv(framed, kernel):
    summed = lax.conv_general_dilated(
        framed[None],
        kernel,
        (1, 1, 1),
        ((0, 0), (0, 0), (1, 1)),
        dimension_numbers=("NDCHW", "ODHWI", "NDCHW"),
        preferred_element_type=jnp.float32,
    )
    return summed[0]


def depth_halo(block, reach):
    count = lax.axis_size("depth")
    forward = [(i, i + 1) for i in range(count - 1)]
    backward = [(i + 1, i) for i in range(count - 1)]
    low = lax.ppermute(block[block.shape[0] - reach :], "depth", forward)
    high = lax.ppermute(block[:reach], "depth", backward)
    return jnp.concatenate([low, block, high], axis=0)


def gather_kernels(first_kernel, second_kernel):
    outs, chans = first_kernel.shape[3], first_kernel.shape[4]
    first = jnp.moveaxis(first_kernel.reshape(27, outs, chans), 1, 0)
    second = jnp.moveaxis(second_kernel.reshape(27, outs, second_kernel.shape[4]), 1, 0)
    whole = lax.all_gather(jnp.concatenate([first, second], axis=2), "filt", axis=0, tiled=True)
    total = whole.shape[0]
    return (
        whole[:, :, :chans].reshape(total, 3, 3, 3, chans),
        whole[:, :, chans:].reshape(total, 3, 3, 3, second_kernel.shape[4]),
    )


def gather_biases(first_bias, second_bias):
    count = lax.axis_size("filt")
    pair = jnp.stack([first_bias, second_bias])
    spread = jnp.broadcast_to(pair[None], (count,) + pair.shape)
    whole = lax.all_to_all(spread, "filt", 0, 0, tiled=True)
    return whole[:, 0].reshape(-1), whole[:, 1].reshape(-1)


def inside(count_planes, count_rows, planes, block_rows):
    plane = lax.axis_index("depth") * planes - 1 + jnp.arange(planes + 2)
    row = lax.axis_index("filt") * block_rows - 1 + jnp.arange(block_rows + 2)
    plane_ok = (plane >= 0) & (plane < count_planes)
    row_ok = (row >= 0) & (row < count_rows)
    return plane_ok[:, None, None, None] & row_ok[None, None, :, None]


def local(features, first_kernel, first_bias, second_kernel, second_bias):
    count = lax.axis_size("filt")
    planes, chans, cells = features.shape
    rows = cells // SIDE
    block_rows = rows // count
    kernel_1, kernel_2 = gather_kernels(first_kernel, second_kernel)
    bias_1, bias_2 = gather_biases(first_bias, second_bias)

    extended = depth_halo(features, 2).reshape(planes + 4, chans, rows, SIDE)
    framed = jnp.pad(extended, ((0, 0), (0, 0), (2, max(2, block_rows)), (0, 0)))
    heads = framed[:, :, :rows].reshape(planes + 4, chans, count, block_rows, SIDE)
    tails = framed[:, :, block_rows : rows + block_rows].reshape(planes + 4, chans, count, block_rows, SIDE)
    windows = jnp.concatenate([heads, tails[:, :, :, : 4]], axis=3)
    windows = windows.reshape(planes + 4, chans, count, (block_rows + 4) * SIDE)
    mine = lax.all_to_all(windows, "filt", 2, 1, tiled=True)
    mine = mine.reshape(planes + 4, count * chans, block_rows + 4, SIDE)

    hidden = activate(conv(mine, kernel_1), bias_1)
    grid = inside(planes * lax.axis_size("depth"), rows, planes, block_rows)
    hidden = jnp.where(grid, hidden, jnp.zeros_like(hidden))
    half = kernel_2.shape[0] // 2
    second = jnp.concatenate([conv(hidden, kernel_2[:half]), conv(hidden, kernel_2[half:])], axis=1)
    second = activate(second, bias_2)

    outs = second_kernel.shape[3]
    second = second.reshape(planes, count, outs, block_rows * SIDE)
    result = lax.all_to_all(second, "filt", 1, 3, tiled=True)
    return result.reshape(planes, outs, cells)


def solution(mesh):
    in_specs = (
        P("depth", "filt", None),
        P(None, None, None, "filt", None),
        P("filt"),
        P(None, None, None, "filt", None),
        P("filt"),
    )
    out_specs = P("depth", "filt", None)
    return jax.shard_map(local, mesh=mesh, in_specs=in_specs, out_specs=out_specs, check_vma=False)
```

```python
import jax
import jax.numpy as jnp
from jax import lax
from jax.sharding import PartitionSpec as P

SIDE = 64


leak_slope = 0.3


def activate(summed, bias):
    shifted = summed + bias[None, :, None, None]
    return jnp.where(shifted > 0, shifted, leak_slope * shifted).astype(jnp.bfloat16)


def conv(framed, kernel):
    summed = lax.conv_general_dilated(
        framed[None],
        kernel,
        (1, 1, 1),
        ((0, 0), (0, 0), (1, 1)),
        dimension_numbers=("NDCHW", "ODHWI", "NDCHW"),
        preferred_element_type=jnp.float32,
    )
    return summed[0]


def depth_halo(block, reach):
    count = lax.axis_size("depth")
    forward = [(i, i + 1) for i in range(count - 1)]
    backward = [(i + 1, i) for i in range(count - 1)]
    low = lax.ppermute(block[block.shape[0] - reach :], "depth", forward)
    high = lax.ppermute(block[:reach], "depth", backward)
    return jnp.concatenate([low, block, high], axis=0)


def gather_kernels(first_kernel, second_kernel):
    outs, chans = first_kernel.shape[3], first_kernel.shape[4]
    first = jnp.moveaxis(first_kernel.reshape(27, outs, chans), 1, 0)
    second = jnp.moveaxis(second_kernel.reshape(27, outs, second_kernel.shape[4]), 1, 0)
    whole = lax.all_gather(jnp.concatenate([first, second], axis=2), "filt", axis=0, tiled=True)
    total = whole.shape[0]
    return (
        whole[:, :, :chans].reshape(total, 3, 3, 3, chans),
        whole[:, :, chans:].reshape(total, 3, 3, 3, second_kernel.shape[4]),
    )


def gather_biases(first_bias, second_bias):
    count = lax.axis_size("filt")
    pair = jnp.stack([first_bias, second_bias])
    spread = jnp.broadcast_to(pair[None], (count,) + pair.shape)
    whole = lax.all_to_all(spread, "filt", 0, 0, tiled=True)
    return whole[:, 0].reshape(-1), whole[:, 1].reshape(-1)


def inside(count_planes, count_rows, planes, block_rows):
    plane = lax.axis_index("depth") * planes - 1 + jnp.arange(planes + 2)
    row = lax.axis_index("filt") * block_rows - 1 + jnp.arange(block_rows + 2)
    plane_ok = (plane >= 0) & (plane < count_planes)
    row_ok = (row >= 0) & (row < count_rows)
    return plane_ok[:, None, None, None] & row_ok[None, None, :, None]


def local(features, first_kernel, first_bias, second_kernel, second_bias):
    count = lax.axis_size("filt")
    planes, chans, cells = features.shape
    rows = cells // SIDE
    block_rows = rows // count
    kernel_1, kernel_2 = gather_kernels(first_kernel, second_kernel)
    bias_1, bias_2 = gather_biases(first_bias, second_bias)

    extended = depth_halo(features, 2).reshape(planes + 4, chans, rows, SIDE)
    framed = jnp.pad(extended, ((0, 0), (0, 0), (2, max(2, block_rows)), (0, 0)))
    heads = framed[:, :, :rows].reshape(planes + 4, chans, count, block_rows, SIDE)
    tails = framed[:, :, block_rows : rows + block_rows].reshape(planes + 4, chans, count, block_rows, SIDE)
    windows = jnp.concatenate([heads, tails[:, :, :, : 4]], axis=3)
    windows = windows.reshape(planes + 4, chans, count, (block_rows + 4) * SIDE)
    mine = lax.all_to_all(windows, "filt", 2, 1, tiled=True)
    mine = mine.reshape(planes + 4, count * chans, block_rows + 4, SIDE)

    count_out = planes + 2
    stacked = jnp.concatenate([mine[i : i + count_out] for i in range(3)], axis=1)
    taps_1 = jnp.transpose(kernel_1, (0, 2, 3, 1, 4)).reshape(kernel_1.shape[0], 3, 3, 3 * kernel_1.shape[4])
    summed_1 = lax.conv_general_dilated(
        stacked,
        taps_1,
        (1, 1),
        ((0, 0), (1, 1)),
        dimension_numbers=("NCHW", "OHWI", "NCHW"),
        preferred_element_type=jnp.float32,
    )
    hidden = activate(summed_1, bias_1)
    grid = inside(planes * lax.axis_size("depth"), rows, planes, block_rows)
    hidden = jnp.where(grid, hidden, jnp.zeros_like(hidden))
    second = activate(conv(hidden, kernel_2), bias_2)

    outs = second_kernel.shape[3]
    second = second.reshape(planes, count, outs, block_rows * SIDE)
    result = lax.all_to_all(second, "filt", 1, 3, tiled=True)
    return result.reshape(planes, outs, cells)


def solution(mesh):
    in_specs = (
        P("depth", "filt", None),
        P(None, None, None, "filt", None),
        P("filt"),
        P(None, None, None, "filt", None),
        P("filt"),
    )
    out_specs = P("depth", "filt", None)
    return jax.shard_map(local, mesh=mesh, in_specs=in_specs, out_specs=out_specs, check_vma=False)
```

```python
import jax
import jax.numpy as jnp
from jax import lax
from jax.sharding import PartitionSpec as P

SIDE = 64


leak_slope = 0.3


def activate(summed, bias):
    shifted = summed + bias[None, :, None, None]
    return jnp.where(shifted > 0, shifted, leak_slope * shifted).astype(jnp.bfloat16)


def conv(framed, kernel):
    summed = lax.conv_general_dilated(
        framed[None],
        kernel,
        (1, 1, 1),
        ((0, 0), (0, 0), (1, 1)),
        dimension_numbers=("NDCHW", "ODHWI", "NDCHW"),
        preferred_element_type=jnp.float32,
    )
    return summed[0]


def depth_halo(block, reach):
    count = lax.axis_size("depth")
    forward = [(i, i + 1) for i in range(count - 1)]
    backward = [(i + 1, i) for i in range(count - 1)]
    low = lax.ppermute(block[block.shape[0] - reach :], "depth", forward)
    high = lax.ppermute(block[:reach], "depth", backward)
    return jnp.concatenate([low, block, high], axis=0)


def gather_kernels(first_kernel, second_kernel):
    outs, chans = first_kernel.shape[3], first_kernel.shape[4]
    first = jnp.moveaxis(first_kernel.reshape(27, outs, chans), 1, 0)
    second = jnp.moveaxis(second_kernel.reshape(27, outs, second_kernel.shape[4]), 1, 0)
    whole = lax.all_gather(jnp.concatenate([first, second], axis=2), "filt", axis=0, tiled=True)
    total = whole.shape[0]
    return (
        whole[:, :, :chans].reshape(total, 3, 3, 3, chans),
        whole[:, :, chans:].reshape(total, 3, 3, 3, second_kernel.shape[4]),
    )


def bias_parts(first_bias, second_bias):
    parts = []
    for bias in (first_bias, second_bias):
        rest = bias
        for _ in range(3):
            piece = rest.astype(jnp.bfloat16)
            parts.append(piece)
            rest = rest - piece.astype(jnp.float32)
    return jnp.stack(parts).reshape(-1)


def joined_biases(received, outs):
    parts = received.astype(jnp.float32).reshape(received.shape[0], 2, 3, outs)
    whole = (parts[:, :, 0] + parts[:, :, 1]) + parts[:, :, 2]
    return whole[:, 0].reshape(-1), whole[:, 1].reshape(-1)


def inside(count_planes, count_rows, planes, block_rows):
    plane = lax.axis_index("depth") * planes - 1 + jnp.arange(planes + 2)
    row = lax.axis_index("filt") * block_rows - 1 + jnp.arange(block_rows + 2)
    plane_ok = (plane >= 0) & (plane < count_planes)
    row_ok = (row >= 0) & (row < count_rows)
    return plane_ok[:, None, None, None] & row_ok[None, None, :, None]


def local(features, first_kernel, first_bias, second_kernel, second_bias):
    count = lax.axis_size("filt")
    planes, chans, cells = features.shape
    rows = cells // SIDE
    block_rows = rows // count
    kernel_1, kernel_2 = gather_kernels(first_kernel, second_kernel)

    extended = depth_halo(features, 2).reshape(planes + 4, chans, rows, SIDE)
    framed = jnp.pad(extended, ((0, 0), (0, 0), (2, max(2, block_rows)), (0, 0)))
    heads = framed[:, :, :rows].reshape(planes + 4, chans, count, block_rows, SIDE)
    tails = framed[:, :, block_rows : rows + block_rows].reshape(planes + 4, chans, count, block_rows, SIDE)
    windows = jnp.concatenate([heads, tails[:, :, :, : 4]], axis=3)
    span = (block_rows + 4) * SIDE
    windows = windows.reshape(planes + 4, chans, count, span)
    parts = bias_parts(first_bias, second_bias)
    extra = jnp.zeros((planes + 4, 1, count, span), jnp.bfloat16)
    extra = extra.at[0, 0, :, : parts.shape[0]].set(jnp.broadcast_to(parts, (count, parts.shape[0])))
    sent = jnp.concatenate([windows, extra], axis=1)
    got = lax.all_to_all(sent, "filt", 2, 1, tiled=True).reshape(planes + 4, count, chans + 1, span)
    bias_1, bias_2 = joined_biases(got[0, :, chans, : parts.shape[0]], first_bias.shape[0])
    mine = got[:, :, :chans].reshape(planes + 4, count * chans, block_rows + 4, SIDE)

    hidden = activate(conv(mine, kernel_1), bias_1)
    grid = inside(planes * lax.axis_size("depth"), rows, planes, block_rows)
    hidden = jnp.where(grid, hidden, jnp.zeros_like(hidden))
    second = activate(conv(hidden, kernel_2), bias_2)

    outs = second_kernel.shape[3]
    second = second.reshape(planes, count, outs, block_rows * SIDE)
    result = lax.all_to_all(second, "filt", 1, 3, tiled=True)
    return result.reshape(planes, outs, cells)


def solution(mesh):
    in_specs = (
        P("depth", "filt", None),
        P(None, None, None, "filt", None),
        P("filt"),
        P(None, None, None, "filt", None),
        P("filt"),
    )
    out_specs = P("depth", "filt", None)
    return jax.shard_map(local, mesh=mesh, in_specs=in_specs, out_specs=out_specs, check_vma=False)
```

```python
import jax
import jax.numpy as jnp
from jax import lax
from jax.sharding import PartitionSpec as P

SIDE = 64


leak_slope = 0.3


def activate(summed, bias):
    shifted = summed + bias[None, :, None, None]
    return jnp.where(shifted > 0, shifted, leak_slope * shifted).astype(jnp.bfloat16)


def conv(framed, kernel):
    summed = lax.conv_general_dilated(
        framed[None],
        kernel,
        (1, 1, 1),
        ((0, 0), (0, 0), (1, 1)),
        dimension_numbers=("NDCHW", "ODHWI", "NDCHW"),
        preferred_element_type=jnp.float32,
    )
    return summed[0]


def depth_halo(block, reach):
    count = lax.axis_size("depth")
    forward = [(i, i + 1) for i in range(count - 1)]
    backward = [(i + 1, i) for i in range(count - 1)]
    low = lax.ppermute(block[block.shape[0] - reach :], "depth", forward)
    high = lax.ppermute(block[:reach], "depth", backward)
    return jnp.concatenate([low, block, high], axis=0)


def gather_kernels(first_kernel, second_kernel):
    outs, chans = first_kernel.shape[3], first_kernel.shape[4]
    first = jnp.moveaxis(first_kernel.reshape(27, outs, chans), 1, 0)
    second = jnp.moveaxis(second_kernel.reshape(27, outs, second_kernel.shape[4]), 1, 0)
    whole = lax.all_gather(jnp.concatenate([first, second], axis=2), "filt", axis=0, tiled=True)
    total = whole.shape[0]
    return (
        whole[:, :, :chans].reshape(total, 3, 3, 3, chans),
        whole[:, :, chans:].reshape(total, 3, 3, 3, second_kernel.shape[4]),
    )


def gather_biases(first_bias, second_bias):
    count = lax.axis_size("filt")
    pair = jnp.stack([first_bias, second_bias])
    spread = jnp.broadcast_to(pair[None], (count,) + pair.shape)
    whole = lax.all_to_all(spread, "filt", 0, 0, tiled=True)
    return whole[:, 0].reshape(-1), whole[:, 1].reshape(-1)


def inside(count_planes, count_rows, planes, block_rows):
    plane = lax.axis_index("depth") * planes - 1 + jnp.arange(planes + 2)
    row = lax.axis_index("filt") * block_rows - 1 + jnp.arange(block_rows + 2)
    plane_ok = (plane >= 0) & (plane < count_planes)
    row_ok = (row >= 0) & (row < count_rows)
    return plane_ok[:, None, None, None] & row_ok[None, None, :, None]


def local(features, first_kernel, first_bias, second_kernel, second_bias):
    count = lax.axis_size("filt")
    planes, chans, cells = features.shape
    rows = cells // SIDE
    block_rows = rows // count
    kernel_1, kernel_2 = gather_kernels(first_kernel, second_kernel)
    bias_1, bias_2 = gather_biases(first_bias, second_bias)

    extended = depth_halo(features, 2).reshape(planes + 4, chans, rows, SIDE)
    framed = jnp.pad(extended, ((0, 0), (0, 0), (2, max(2, block_rows)), (0, 0)))
    heads = framed[:, :, :rows].reshape(planes + 4, chans, count, block_rows, SIDE)
    tails = framed[:, :, block_rows : rows + block_rows].reshape(planes + 4, chans, count, block_rows, SIDE)
    windows = jnp.concatenate([heads, tails[:, :, :, : 4]], axis=3)
    windows = windows.reshape(planes + 4, chans, count, (block_rows + 4) * SIDE)
    mine = lax.all_to_all(windows, "filt", 2, 1, tiled=True)
    mine = mine.reshape(planes + 4, count * chans, block_rows + 4, SIDE)

    hidden = activate(conv(mine, kernel_1), bias_1)
    grid = inside(planes * lax.axis_size("depth"), rows, planes, block_rows)
    hidden = jnp.where(grid, hidden, jnp.zeros_like(hidden))
    half = kernel_2.shape[0] // 2
    pieces = lax.optimization_barrier((kernel_2[:half], kernel_2[half:]))
    second = activate(conv(hidden, jnp.concatenate(pieces, axis=0)), bias_2)

    outs = second_kernel.shape[3]
    second = second.reshape(planes, count, outs, block_rows * SIDE)
    result = lax.all_to_all(second, "filt", 1, 3, tiled=True)
    return result.reshape(planes, outs, cells)


def solution(mesh):
    in_specs = (
        P("depth", "filt", None),
        P(None, None, None, "filt", None),
        P("filt"),
        P(None, None, None, "filt", None),
        P("filt"),
    )
    out_specs = P("depth", "filt", None)
    return jax.shard_map(local, mesh=mesh, in_specs=in_specs, out_specs=out_specs, check_vma=False)
```

```python
import jax
import jax.numpy as jnp
from jax import lax
from jax.sharding import PartitionSpec as P

SIDE = 64


leak_slope = 0.3


def activate(summed, bias):
    shifted = summed + bias[None, :, None, None]
    return jnp.where(shifted > 0, shifted, leak_slope * shifted).astype(jnp.bfloat16)


def conv(framed, kernel):
    summed = lax.conv_general_dilated(
        framed[None],
        kernel,
        (1, 1, 1),
        ((0, 0), (0, 0), (1, 1)),
        dimension_numbers=("NDCHW", "ODHWI", "NDCHW"),
        preferred_element_type=jnp.float32,
    )
    return summed[0]


def depth_halo(block, reach):
    count = lax.axis_size("depth")
    forward = [(i, i + 1) for i in range(count - 1)]
    backward = [(i + 1, i) for i in range(count - 1)]
    low = lax.ppermute(block[block.shape[0] - reach :], "depth", forward)
    high = lax.ppermute(block[:reach], "depth", backward)
    return jnp.concatenate([low, block, high], axis=0)


def gather_kernels(first_kernel, second_kernel):
    outs, chans = first_kernel.shape[3], first_kernel.shape[4]
    first = jnp.moveaxis(first_kernel.reshape(27, outs, chans), 1, 0)
    second = jnp.moveaxis(second_kernel.reshape(27, outs, second_kernel.shape[4]), 1, 0)
    whole = lax.all_gather(jnp.concatenate([first, second], axis=2), "filt", axis=0, tiled=True)
    total = whole.shape[0]
    return (
        whole[:, :, :chans].reshape(total, 3, 3, 3, chans),
        whole[:, :, chans:].reshape(total, 3, 3, 3, second_kernel.shape[4]),
    )


def gather_biases(first_bias, second_bias):
    count = lax.axis_size("filt")
    pair = jnp.stack([first_bias, second_bias])
    spread = jnp.broadcast_to(pair[None], (count,) + pair.shape)
    whole = lax.all_to_all(spread, "filt", 0, 0, tiled=True)
    return whole[:, 0].reshape(-1), whole[:, 1].reshape(-1)


def inside(count_planes, count_rows, planes, block_rows):
    plane = lax.axis_index("depth") * planes - 1 + jnp.arange(planes + 2)
    row = lax.axis_index("filt") * block_rows - 1 + jnp.arange(block_rows + 2)
    plane_ok = (plane >= 0) & (plane < count_planes)
    row_ok = (row >= 0) & (row < count_rows)
    return plane_ok[:, None, None, None] & row_ok[None, None, :, None]


def local(features, first_kernel, first_bias, second_kernel, second_bias):
    count = lax.axis_size("filt")
    planes, chans, cells = features.shape
    rows = cells // SIDE
    block_rows = rows // count
    kernel_1, kernel_2 = gather_kernels(first_kernel, second_kernel)
    bias_1, bias_2 = gather_biases(first_bias, second_bias)

    extended = depth_halo(features, 2).reshape(planes + 4, chans, rows, SIDE)
    framed = jnp.pad(extended, ((0, 0), (0, 0), (2, max(2, block_rows)), (0, 0)))
    heads = framed[:, :, :rows].reshape(planes + 4, chans, count, block_rows, SIDE)
    tails = framed[:, :, block_rows : rows + block_rows].reshape(planes + 4, chans, count, block_rows, SIDE)
    windows = jnp.concatenate([heads, tails[:, :, :, : 4]], axis=3)
    windows = windows.reshape(planes + 4, chans, count, (block_rows + 4) * SIDE)
    mine = lax.all_to_all(windows, "filt", 2, 1, tiled=True)
    mine = mine.reshape(planes + 4, count * chans, block_rows + 4, SIDE)

    half_1 = kernel_1.shape[0] // 2
    pieces_1 = lax.optimization_barrier((kernel_1[:half_1], kernel_1[half_1:]))
    hidden = activate(conv(mine, jnp.concatenate(pieces_1, axis=0)), bias_1)
    grid = inside(planes * lax.axis_size("depth"), rows, planes, block_rows)
    hidden = jnp.where(grid, hidden, jnp.zeros_like(hidden))
    half = kernel_2.shape[0] // 2
    pieces = lax.optimization_barrier((kernel_2[:half], kernel_2[half:]))
    second = activate(conv(hidden, jnp.concatenate(pieces, axis=0)), bias_2)

    outs = second_kernel.shape[3]
    second = second.reshape(planes, count, outs, block_rows * SIDE)
    result = lax.all_to_all(second, "filt", 1, 3, tiled=True)
    return result.reshape(planes, outs, cells)


def solution(mesh):
    in_specs = (
        P("depth", "filt", None),
        P(None, None, None, "filt", None),
        P("filt"),
        P(None, None, None, "filt", None),
        P("filt"),
    )
    out_specs = P("depth", "filt", None)
    return jax.shard_map(local, mesh=mesh, in_specs=in_specs, out_specs=out_specs, check_vma=False)
```
